256 devices in a mesh: ctx: 32 (over y, z), tp: 8 (over x, core).
Axes of the slice: x: 4, y: 4, z: 8, core: 2. Of those that a mesh axis runs over, the one named last changes fastest.
Arguments:
- queries: bfloat16 [32768, 4096], P('ctx', 'tp'), may hold values from -6 to 6
- keys: bfloat16 [32768, 4096], P('ctx', 'tp'), may hold values from -6 to 6
- values: bfloat16 [32768, 4096], P('ctx', 'tp'), may hold values from -128 to 128
- gates: bfloat16 [32768, 4096], P('ctx', 'tp'), may hold values from -6 to 6
- log_decay: float32 [32, 32768], P('tp', 'ctx'), may hold values from -1 to 0, as said below
- norm_gain: float32 [4096], P('tp'), may hold values from 0.1 to 1.9
- out_weight: bfloat16 [4096, 6144], P('tp'), may hold values from -0.09375 to 0.09375
Outputs:
- attended: bfloat16 [32768, 6144], P(('ctx', 'tp'))
The draws below stay inside these ranges and needn't reach their ends.
Inputs may be any that keep to these rules, and one draw needn't show every extreme that they name: log_decay is negative everywhere.
All inputs are finite; a program needn't handle non-finite values.
Results may differ from the reference program's by a relative error of at most 0.017.
Values may be sent and summed in bfloat16 or wider, within the bound.
No kernel may reach another device: no remote copies, remote signals or barrier semaphores. Data moves between devices by JAX's collectives and lax.ppermute only.
A program may use at most 64 MiB of HBM per device.

```python
import math
import jax
import jax.numpy as jnp
from jax import lax

D = 6144
SHARD_ATTENDERS = 32
DH = 128
T_DEV = 1024
SPAN_ELEMENTS = 32768
HL = 4


def draw_values(key, part):
    key_base, key_col, key_row = jax.random.split(key, 3)
    base = jnp.clip(jax.random.normal(key_base, (SPAN_ELEMENTS, SHARD_ATTENDERS * DH), jnp.float32), -4.0, 4.0)
    upper = math.log(10.0)
    col_scale = jnp.exp(jax.random.uniform(key_col, (1, SHARD_ATTENDERS * DH), jnp.float32, 0.0, upper))
    row_scale = jnp.exp(jax.random.uniform(key_row, (SPAN_ELEMENTS, 1), jnp.float32, 0.0, math.log(2.0)))
    return (base * col_scale * row_scale).astype(jnp.bfloat16)


def draw_log_decay(key, part):
    complete_lookup_matrix = jax.random.split(key, 7)
    slow_share = 0.5
    slow_pick = jax.random.uniform(complete_lookup_matrix[0], (SHARD_ATTENDERS, 1), jnp.float32) < slow_share
    slow_rate = jnp.exp(jax.random.uniform(complete_lookup_matrix[1], (SHARD_ATTENDERS, 1), jnp.float32, math.log(0.05 / SPAN_ELEMENTS), math.log(0.4 / SPAN_ELEMENTS)))
    fast_rate = jnp.exp(jax.random.uniform(complete_lookup_matrix[2], (SHARD_ATTENDERS, 1), jnp.float32, math.log(1.0 / 50.0), math.log(1.0 / 30.0)))
    base_rate = jnp.where(slow_pick, slow_rate, fast_rate)
    block_count = SPAN_ELEMENTS // T_DEV
    factor = jnp.exp(jax.random.uniform(complete_lookup_matrix[3], (SHARD_ATTENDERS, block_count, 1), jnp.float32, math.log(0.5), math.log(2.0)))
    rate = jnp.broadcast_to(base_rate[:, :, None] * factor, (SHARD_ATTENDERS, block_count, T_DEV)).reshape(SHARD_ATTENDERS, SPAN_ELEMENTS)
    first_offset = jax.random.randint(complete_lookup_matrix[4], (SHARD_ATTENDERS, 1), 0, SPAN_ELEMENTS)
    offset_gap = jax.random.randint(complete_lookup_matrix[6], (SHARD_ATTENDERS, 1), 1, SPAN_ELEMENTS)
    second_offset = (first_offset + offset_gap) % SPAN_ELEMENTS
    segment_offset = jnp.concatenate([first_offset, second_offset], axis=1)
    element_indices = jnp.arange(SPAN_ELEMENTS)
    agreement_tally = jnp.sum((element_indices[None, None, :] == segment_offset[:, :, None]).astype(jnp.float32), axis=1)
    loss = jnp.log(jax.random.uniform(complete_lookup_matrix[5], (SHARD_ATTENDERS, SPAN_ELEMENTS), jnp.float32, 0.5, 0.8))
    return -rate + agreement_tally * loss


def levels(stream_key, shape, pieces, least, high):
    def one(axis_at, blocks):
        draws = jax.random.uniform(jax.random.fold_in(jax.random.fold_in(stream_key, 6), axis_at), (blocks,), jnp.float32, least / len(pieces), high / len(pieces))
        return jnp.repeat(jnp.exp(draws), shape[axis_at] // blocks).reshape((-1,) + (1,) * (len(shape) - axis_at - 1))

    factor_of = one(*pieces[0])
    for cut in pieces[1:]:
        factor_of = factor_of * one(*cut)
    return factor_of


def centred(own_key, extent, width, reach, pieces=(), held_as=jnp.bfloat16):
    drawn = width * jax.random.normal(own_key, extent, jnp.float32)
    if pieces:
        drawn = drawn * levels(own_key, extent, pieces, -0.22, 0.18)
    return jnp.clip(drawn, -reach, reach).astype(held_as)


def setup_inputs(seed: int = 0) -> dict:
    splits = jax.random.split(jax.random.key(seed), 8)
    queries = centred(splits[0], (SPAN_ELEMENTS, SHARD_ATTENDERS * DH), 1.0, 6.0, ((0, 32), (1, 8)))
    keys = centred(splits[1], (SPAN_ELEMENTS, SHARD_ATTENDERS * DH), 1.0, 6.0, ((0, 32), (1, 8)))
    values = draw_values(jax.random.fold_in(splits[7], 71), 0)
    gates = centred(splits[3], (SPAN_ELEMENTS, SHARD_ATTENDERS * DH), 1.5, 6.0, ((0, 32), (1, 8)))
    log_decay = draw_log_decay(jax.random.fold_in(splits[7], 71), 0)
    norm_gain = jnp.clip(1.0 + 0.18 * jax.random.normal(splits[5], (SHARD_ATTENDERS * DH,), jnp.float32), 0.1, 1.9)
    out_weight = centred(splits[6], (SHARD_ATTENDERS * DH, D), (SHARD_ATTENDERS * DH) ** -0.5, 0.09375, ((0, 8),))
    return dict(queries=queries, keys=keys, values=values, gates=gates, log_decay=log_decay, norm_gain=norm_gain, out_weight=out_weight)


def block_step(carry_state, block_inputs):
    query_blk, key_blk, value_blk, block_decay_factor = block_inputs
    query_full = query_blk.astype(jnp.float32)
    key_full = key_blk.astype(jnp.float32)
    value_full = value_blk.astype(jnp.float32)
    block_cum = jnp.cumsum(block_decay_factor, axis=1)
    width_blk = block_decay_factor.shape[1]
    lower = jnp.arange(width_blk)[:, None] >= jnp.arange(width_blk)[None, :]
    spread = block_cum[:, :, None] - block_cum[:, None, :]
    factor = jnp.exp(jnp.where(lower[None], spread, -jnp.inf))
    scores = jnp.einsum('thd,shd->hts', query_full, key_full, precision=lax.Precision.HIGHEST)
    weighted = (scores * factor).astype(jnp.bfloat16)
    inside = jnp.einsum('hts,shd->thd', weighted.astype(jnp.float32), value_full, precision=lax.Precision.HIGHEST)
    carried = jnp.exp(block_cum).T[:, :, None] * jnp.einsum('thd,hde->the', query_full, carry_state, precision=lax.Precision.HIGHEST)
    tail = jnp.exp(block_cum[:, -1:] - block_cum)
    key_decayed = key_full * tail.T[:, :, None]
    new_state = jnp.exp(block_cum[:, -1])[:, None, None] * carry_state + jnp.einsum('shd,she->hde', key_decayed, value_full, precision=lax.Precision.HIGHEST)
    return (new_state, inside + carried)

def reference(queries, keys, values, gates, log_decay, norm_gain, out_weight):
    width_blk = min(T_DEV, 512)
    blocks = SPAN_ELEMENTS // width_blk
    query_r = queries.reshape(blocks, width_blk, SHARD_ATTENDERS, DH)
    key_r = keys.reshape(blocks, width_blk, SHARD_ATTENDERS, DH)
    value_r = values.reshape(blocks, width_blk, SHARD_ATTENDERS, DH)
    decay_r = log_decay.reshape(SHARD_ATTENDERS, blocks, width_blk).transpose(1, 0, 2)
    start_state = jnp.zeros((SHARD_ATTENDERS, DH, DH), jnp.float32)
    final_state, attn = lax.scan(block_step, start_state, (query_r, key_r, value_r, decay_r))
    attn = attn.reshape(SPAN_ELEMENTS, SHARD_ATTENDERS, DH)
    meansq = lax.optimization_barrier(jnp.mean(attn * attn, axis=-1, keepdims=True))
    entire_gating_vector = jax.nn.sigmoid(gates.reshape(SPAN_ELEMENTS, SHARD_ATTENDERS, DH).astype(jnp.float32))
    normed = attn * lax.rsqrt(meansq + 1e-06) * norm_gain.reshape(SHARD_ATTENDERS, DH) * entire_gating_vector
    normed = normed.astype(jnp.bfloat16).reshape(SPAN_ELEMENTS, SHARD_ATTENDERS * DH)
    group_cols = HL * DH
    total = jnp.zeros((SPAN_ELEMENTS, D), jnp.float32)
    for group in range(SHARD_ATTENDERS // HL):
        incomplete_addition = jnp.dot(normed[:, group * group_cols:(group + 1) * group_cols], out_weight[group * group_cols:(group + 1) * group_cols], preferred_element_type=jnp.float32).astype(jnp.bfloat16)
        incomplete_addition = lax.optimization_barrier(incomplete_addition)
        total = total + incomplete_addition.astype(jnp.float32)
    return total.astype(jnp.bfloat16)
```

```python
import jax
import jax.numpy as jnp
from jax import lax
from jax.sharding import PartitionSpec as P


def chain_join(earlier, later):
    return (jnp.exp(later[1])[:, None, None] * earlier[0] + later[0], earlier[1] + later[1])


def exclusive_prefix(state, total, axis):
    n = lax.axis_size(axis)

    def shifted(x, s):
        return lax.ppermute(x, axis, [(i, i + s) for i in range(n - s)])

    acc = (shifted(state, 1), shifted(total, 1))
    s = 1
    while s < n:
        got = (shifted(acc[0], s), shifted(acc[1], s))
        acc = chain_join(got, acc)
        s *= 2
    return acc[0]


def on_device(queries, keys, values, gates, log_decay, norm_gain, out_weight):
    local_rows = queries.shape[0]
    head_count = log_decay.shape[0]
    head_width = queries.shape[1] // head_count
    width_blk = min(local_rows, 512)
    blocks = local_rows // width_blk
    hp = lax.Precision.HIGHEST

    q = queries.reshape(blocks, width_blk, head_count, head_width)
    k = keys.reshape(blocks, width_blk, head_count, head_width)
    v = values.reshape(blocks, width_blk, head_count, head_width)
    decay = log_decay.reshape(head_count, blocks, width_blk).transpose(1, 0, 2)
    cum = jnp.cumsum(decay, axis=2)
    last = cum[:, :, -1]

    tail = jnp.exp(last[:, :, None] - cum)
    key_decayed = k.astype(jnp.float32) * tail.transpose(0, 2, 1)[:, :, :, None]
    block_state = jnp.einsum(
        "bshd,bshe->bhde", key_decayed, v.astype(jnp.float32), precision=hp
    )

    carries = []
    run = jnp.zeros((head_count, head_width, head_width), jnp.float32)
    before = jnp.zeros((head_count,), jnp.float32)
    offsets = []
    for b in range(blocks):
        carries.append(run)
        offsets.append(before)
        run = jnp.exp(last[b])[:, None, None] * run + block_state[b]
        before = before + last[b]
    local_state = run
    own_total = before

    incoming = exclusive_prefix(local_state, own_total, "ctx")

    lower = jnp.arange(width_blk)[:, None] >= jnp.arange(width_blk)[None, :]
    spread = cum[:, :, :, None] - cum[:, :, None, :]
    factor = jnp.exp(jnp.where(lower[None, None], spread, -jnp.inf))
    scores = jnp.einsum("bthd,bshd->bhts", q, k, preferred_element_type=jnp.float32)
    weighted = (scores * factor).astype(jnp.bfloat16)
    inside = jnp.einsum("bhts,bshd->bthd", weighted, v, preferred_element_type=jnp.float32)

    carry_all = jnp.stack(
        [carries[b] + jnp.exp(offsets[b])[:, None, None] * incoming for b in range(blocks)]
    )
    carried = jnp.exp(cum).transpose(0, 2, 1)[:, :, :, None] * jnp.einsum(
        "bthd,bhde->bthe", q.astype(jnp.float32), carry_all, precision=hp
    )
    attn = (inside + carried).reshape(local_rows, head_count, head_width)

    meansq = jnp.mean(attn * attn, axis=-1, keepdims=True)
    gate = jax.nn.sigmoid(gates.reshape(local_rows, head_count, head_width).astype(jnp.float32))
    normed = attn * lax.rsqrt(meansq + 1e-06) * norm_gain.reshape(head_count, head_width) * gate
    normed = normed.astype(jnp.bfloat16).reshape(local_rows, head_count * head_width)
    return lax.psum_scatter(
        jnp.dot(normed, out_weight, preferred_element_type=jnp.float32).astype(jnp.bfloat16),
        "tp",
        scatter_dimension=0,
        tiled=True,
    )


def solution(mesh):
    placed = (
        P("ctx", "tp"),
        P("ctx", "tp"),
        P("ctx", "tp"),
        P("ctx", "tp"),
        P("tp", "ctx"),
        P("tp"),
        P("tp", None),
    )
    return jax.shard_map(
        on_device, mesh=mesh, in_specs=placed, out_specs=P(("ctx", "tp"), None), check_vma=False
    )
```

```python
import jax
import jax.numpy as jnp
from jax import lax
from jax.sharding import PartitionSpec as P


def exclusive_prefix(state, total, axis):
    n = lax.axis_size(axis)
    heads, rows, cols = state.shape
    pad = 8
    packed = jnp.concatenate(
        [state, jnp.broadcast_to(total[:, None, None], (heads, pad, cols))], axis=1
    )
    is_state = (jnp.arange(rows + pad) < rows)[None, :, None]

    def shifted(x, s):
        return lax.ppermute(x, axis, [(i, i + s) for i in range(n - s)])

    acc = shifted(packed, 1)
    s = 1
    while s < n:
        got = shifted(acc, s)
        scale = jnp.where(is_state, jnp.exp(acc[:, rows : rows + 1, 0:1]), 1.0)
        acc = got * scale + acc
        s *= 2
    return acc[:, :rows, :]


def on_device(queries, keys, values, gates, log_decay, norm_gain, out_weight):
    local_rows = queries.shape[0]
    head_count = log_decay.shape[0]
    head_width = queries.shape[1] // head_count
    width_blk = min(local_rows, 512)
    blocks = local_rows // width_blk
    hp = lax.Precision.HIGHEST

    q = queries.reshape(blocks, width_blk, head_count, head_width)
    k = keys.reshape(blocks, width_blk, head_count, head_width)
    v = values.reshape(blocks, width_blk, head_count, head_width)
    decay = log_decay.reshape(head_count, blocks, width_blk).transpose(1, 0, 2)
    cum = jnp.cumsum(decay, axis=2)
    last = cum[:, :, -1]

    tail = jnp.exp(last[:, :, None] - cum)
    key_decayed = k.astype(jnp.float32) * tail.transpose(0, 2, 1)[:, :, :, None]
    block_state = jnp.einsum(
        "bshd,bshe->bhde", key_decayed, v.astype(jnp.float32), precision=hp
    )

    carries = []
    run = jnp.zeros((head_count, head_width, head_width), jnp.float32)
    before = jnp.zeros((head_count,), jnp.float32)
    offsets = []
    for b in range(blocks):
        carries.append(run)
        offsets.append(before)
        run = jnp.exp(last[b])[:, None, None] * run + block_state[b]
        before = before + last[b]
    local_state = run
    own_total = before

    incoming = exclusive_prefix(local_state, own_total, "ctx")

    lower = jnp.arange(width_blk)[:, None] >= jnp.arange(width_blk)[None, :]
    spread = cum[:, :, :, None] - cum[:, :, None, :]
    factor = jnp.exp(jnp.where(lower[None, None], spread, -jnp.inf))
    scores = jnp.einsum("bthd,bshd->bhts", q, k, preferred_element_type=jnp.float32)
    weighted = (scores * factor).astype(jnp.bfloat16)
    inside = jnp.einsum("bhts,bshd->bthd", weighted, v, preferred_element_type=jnp.float32)

    carry_all = jnp.stack(
        [carries[b] + jnp.exp(offsets[b])[:, None, None] * incoming for b in range(blocks)]
    )
    carried = jnp.exp(cum).transpose(0, 2, 1)[:, :, :, None] * jnp.einsum(
        "bthd,bhde->bthe", q.astype(jnp.float32), carry_all, precision=hp
    )
    attn = (inside + carried).reshape(local_rows, head_count, head_width)

    meansq = jnp.mean(attn * attn, axis=-1, keepdims=True)
    gate = jax.nn.sigmoid(gates.reshape(local_rows, head_count, head_width).astype(jnp.float32))
    normed = attn * lax.rsqrt(meansq + 1e-06) * norm_gain.reshape(head_count, head_width) * gate
    normed = normed.astype(jnp.bfloat16).reshape(local_rows, head_count * head_width)
    return lax.psum_scatter(
        jnp.dot(normed, out_weight, preferred_element_type=jnp.float32).astype(jnp.bfloat16),
        "tp",
        scatter_dimension=0,
        tiled=True,
    )


def solution(mesh):
    placed = (
        P("ctx", "tp"),
        P("ctx", "tp"),
        P("ctx", "tp"),
        P("ctx", "tp"),
        P("tp", "ctx"),
        P("tp"),
        P("tp", None),
    )
    return jax.shard_map(
        on_device, mesh=mesh, in_specs=placed, out_specs=P(("ctx", "tp"), None), check_vma=False
    )
```

```python
import jax
import jax.numpy as jnp
from jax import lax
from jax.sharding import PartitionSpec as P


def exclusive_prefix(state, total, axis):
    n = lax.axis_size(axis)
    heads, rows, cols = state.shape
    pad = 8

    def pack(st, tot):
        hi = tot.astype(jnp.bfloat16)
        lo = (tot - hi.astype(jnp.float32)).astype(jnp.bfloat16)
        parts = jnp.stack([hi, lo] + [jnp.zeros_like(hi)] * (pad - 2), axis=1)
        return jnp.concatenate(
            [st.astype(jnp.bfloat16), jnp.broadcast_to(parts[:, :, None], (heads, pad, cols))],
            axis=1,
        )

    def unpack(x):
        x = x.astype(jnp.float32)
        return x[:, :rows, :], x[:, rows, 0] + x[:, rows + 1, 0]

    def shifted(x, s):
        return lax.ppermute(x, axis, [(i, i + s) for i in range(n - s)])

    st, tot = unpack(shifted(pack(state, total), 1))
    s = 1
    while s < n:
        got_st, got_tot = unpack(shifted(pack(st, tot), s))
        st = jnp.exp(tot)[:, None, None] * got_st + st
        tot = got_tot + tot
        s *= 2
    return st


def on_device(queries, keys, values, gates, log_decay, norm_gain, out_weight):
    local_rows = queries.shape[0]
    head_count = log_decay.shape[0]
    head_width = queries.shape[1] // head_count
    width_blk = min(local_rows, 512)
    blocks = local_rows // width_blk
    hp = lax.Precision.HIGHEST

    q = queries.reshape(blocks, width_blk, head_count, head_width)
    k = keys.reshape(blocks, width_blk, head_count, head_width)
    v = values.reshape(blocks, width_blk, head_count, head_width)
    decay = log_decay.reshape(head_count, blocks, width_blk).transpose(1, 0, 2)
    cum = jnp.cumsum(decay, axis=2)
    last = cum[:, :, -1]

    tail = jnp.exp(last[:, :, None] - cum)
    key_decayed = k.astype(jnp.float32) * tail.transpose(0, 2, 1)[:, :, :, None]
    block_state = jnp.einsum(
        "bshd,bshe->bhde", key_decayed, v.astype(jnp.float32), precision=hp
    )

    carries = []
    run = jnp.zeros((head_count, head_width, head_width), jnp.float32)
    before = jnp.zeros((head_count,), jnp.float32)
    offsets = []
    for b in range(blocks):
        carries.append(run)
        offsets.append(before)
        run = jnp.exp(last[b])[:, None, None] * run + block_state[b]
        before = before + last[b]
    local_state = run
    own_total = before

    incoming = exclusive_prefix(local_state, own_total, "ctx")

    lower = jnp.arange(width_blk)[:, None] >= jnp.arange(width_blk)[None, :]
    spread = cum[:, :, :, None] - cum[:, :, None, :]
    factor = jnp.exp(jnp.where(lower[None, None], spread, -jnp.inf))
    scores = jnp.einsum("bthd,bshd->bhts", q, k, preferred_element_type=jnp.float32)
    weighted = (scores * factor).astype(jnp.bfloat16)
    inside = jnp.einsum("bhts,bshd->bthd", weighted, v, preferred_element_type=jnp.float32)

    carry_all = jnp.stack(
        [carries[b] + jnp.exp(offsets[b])[:, None, None] * incoming for b in range(blocks)]
    )
    carried = jnp.exp(cum).transpose(0, 2, 1)[:, :, :, None] * jnp.einsum(
        "bthd,bhde->bthe", q.astype(jnp.float32), carry_all, precision=hp
    )
    attn = (inside + carried).reshape(local_rows, head_count, head_width)

    meansq = jnp.mean(attn * attn, axis=-1, keepdims=True)
    gate = jax.nn.sigmoid(gates.reshape(local_rows, head_count, head_width).astype(jnp.float32))
    normed = attn * lax.rsqrt(meansq + 1e-06) * norm_gain.reshape(head_count, head_width) * gate
    normed = normed.astype(jnp.bfloat16).reshape(local_rows, head_count * head_width)
    return lax.psum_scatter(
        jnp.dot(normed, out_weight, preferred_element_type=jnp.float32).astype(jnp.bfloat16),
        "tp",
        scatter_dimension=0,
        tiled=True,
    )


def solution(mesh):
    placed = (
        P("ctx", "tp"),
        P("ctx", "tp"),
        P("ctx", "tp"),
        P("ctx", "tp"),
        P("tp", "ctx"),
        P("tp"),
        P("tp", None),
    )
    return jax.shard_map(
        on_device, mesh=mesh, in_specs=placed, out_specs=P(("ctx", "tp"), None), check_vma=False
    )
```

```python
import jax
import jax.numpy as jnp
from jax import lax
from jax.sharding import PartitionSpec as P


def exclusive_prefix(state, total, axis):
    n = lax.axis_size(axis)
    me = lax.axis_index(axis)
    heads, rows, cols = state.shape
    pad = 8

    def pack(st, tot):
        hi = tot.astype(jnp.bfloat16)
        lo = (tot - hi.astype(jnp.float32)).astype(jnp.bfloat16)
        parts = jnp.stack([hi, lo] + [jnp.zeros_like(hi)] * (pad - 2), axis=1)
        return jnp.concatenate(
            [st.astype(jnp.bfloat16), jnp.broadcast_to(parts[:, :, None], (heads, pad, cols))],
            axis=1,
        )

    def unpack(x):
        x = x.astype(jnp.float32)
        return x[:, :rows, :], x[:, rows, 0] + x[:, rows + 1, 0]

    def join(earlier, later):
        return (jnp.exp(later[1])[:, None, None] * earlier[0] + later[0], earlier[1] + later[1])

    block = (state, total)
    prefix = (jnp.zeros_like(state), jnp.zeros_like(total))
    s = 1
    while s < n:
        other = unpack(lax.ppermute(pack(*block), axis, [(i, i ^ s) for i in range(n)]))
        lower = (me & s) != 0
        new_prefix = join(other, prefix)
        prefix = tuple(jnp.where(lower, a, b) for a, b in zip(new_prefix, prefix))
        block = tuple(
            jnp.where(lower, a, b) for a, b in zip(join(other, block), join(block, other))
        )
        s *= 2
    return prefix[0]


def on_device(queries, keys, values, gates, log_decay, norm_gain, out_weight):
    local_rows = queries.shape[0]
    head_count = log_decay.shape[0]
    head_width = queries.shape[1] // head_count
    width_blk = min(local_rows, 512)
    blocks = local_rows // width_blk
    hp = lax.Precision.HIGHEST

    q = queries.reshape(blocks, width_blk, head_count, head_width)
    k = keys.reshape(blocks, width_blk, head_count, head_width)
    v = values.reshape(blocks, width_blk, head_count, head_width)
    decay = log_decay.reshape(head_count, blocks, width_blk).transpose(1, 0, 2)
    cum = jnp.cumsum(decay, axis=2)
    last = cum[:, :, -1]

    tail = jnp.exp(last[:, :, None] - cum)
    key_decayed = k.astype(jnp.float32) * tail.transpose(0, 2, 1)[:, :, :, None]
    block_state = jnp.einsum(
        "bshd,bshe->bhde", key_decayed, v.astype(jnp.float32), precision=hp
    )

    carries = []
    run = jnp.zeros((head_count, head_width, head_width), jnp.float32)
    before = jnp.zeros((head_count,), jnp.float32)
    offsets = []
    for b in range(blocks):
        carries.append(run)
        offsets.append(before)
        run = jnp.exp(last[b])[:, None, None] * run + block_state[b]
        before = before + last[b]
    local_state = run
    own_total = before

    incoming = exclusive_prefix(local_state, own_total, "ctx")

    lower = jnp.arange(width_blk)[:, None] >= jnp.arange(width_blk)[None, :]
    spread = cum[:, :, :, None] - cum[:, :, None, :]
    factor = jnp.exp(jnp.where(lower[None, None], spread, -jnp.inf))
    scores = jnp.einsum("bthd,bshd->bhts", q, k, preferred_element_type=jnp.float32)
    weighted = (scores * factor).astype(jnp.bfloat16)
    inside = jnp.einsum("bhts,bshd->bthd", weighted, v, preferred_element_type=jnp.float32)

    carry_all = jnp.stack(
        [carries[b] + jnp.exp(offsets[b])[:, None, None] * incoming for b in range(blocks)]
    )
    carried = jnp.exp(cum).transpose(0, 2, 1)[:, :, :, None] * jnp.einsum(
        "bthd,bhde->bthe", q.astype(jnp.float32), carry_all, precision=hp
    )
    attn = (inside + carried).reshape(local_rows, head_count, head_width)

    meansq = jnp.mean(attn * attn, axis=-1, keepdims=True)
    gate = jax.nn.sigmoid(gates.reshape(local_rows, head_count, head_width).astype(jnp.float32))
    normed = attn * lax.rsqrt(meansq + 1e-06) * norm_gain.reshape(head_count, head_width) * gate
    normed = normed.astype(jnp.bfloat16).reshape(local_rows, head_count * head_width)
    return lax.psum_scatter(
        jnp.dot(normed, out_weight, preferred_element_type=jnp.float32).astype(jnp.bfloat16),
        "tp",
        scatter_dimension=0,
        tiled=True,
    )


def solution(mesh):
    placed = (
        P("ctx", "tp"),
        P("ctx", "tp"),
        P("ctx", "tp"),
        P("ctx", "tp"),
        P("tp", "ctx"),
        P("tp"),
        P("tp", None),
    )
    return jax.shard_map(
        on_device, mesh=mesh, in_specs=placed, out_specs=P(("ctx", "tp"), None), check_vma=False
    )
```

```python
import jax
import jax.numpy as jnp
from jax import lax
from jax.sharding import PartitionSpec as P


def exclusive_prefix(state, total, axis):
    n = lax.axis_size(axis)
    me = lax.axis_index(axis)
    heads, rows, cols = state.shape
    pad = 8

    def pack(st, tot):
        hi = tot.astype(jnp.bfloat16)
        lo = (tot - hi.astype(jnp.float32)).astype(jnp.bfloat16)
        parts = jnp.stack([hi, lo] + [jnp.zeros_like(hi)] * (pad - 2), axis=1)
        return jnp.concatenate(
            [st.astype(jnp.bfloat16), jnp.broadcast_to(parts[:, :, None], (heads, pad, cols))],
            axis=1,
        )

    def unpack(x):
        x = x.astype(jnp.float32)
        return x[:, :rows, :], x[:, rows, 0] + x[:, rows + 1, 0]

    def join(earlier, later):
        return (jnp.exp(later[1])[:, None, None] * earlier[0] + later[0], earlier[1] + later[1])

    block = (state, total)
    prefix = (jnp.zeros_like(state), jnp.zeros_like(total))
    s = 1
    while s < n:
        other = unpack(lax.ppermute(pack(*block), axis, [(i, i ^ s) for i in range(n)]))
        lower = (me & s) != 0
        new_prefix = join(other, prefix)
        prefix = tuple(jnp.where(lower, a, b) for a, b in zip(new_prefix, prefix))
        block = tuple(
            jnp.where(lower, a, b) for a, b in zip(join(other, block), join(block, other))
        )
        s *= 2
    return prefix[0]


def on_device(queries, keys, values, gates, log_decay, norm_gain, out_weight):
    local_rows = queries.shape[0]
    head_count = log_decay.shape[0]
    head_width = queries.shape[1] // head_count
    width_blk = min(local_rows, 512)
    blocks = local_rows // width_blk
    hp = lax.Precision.HIGHEST

    q = queries.reshape(blocks, width_blk, head_count, head_width)
    k = keys.reshape(blocks, width_blk, head_count, head_width)
    v = values.reshape(blocks, width_blk, head_count, head_width)
    decay = log_decay.reshape(head_count, blocks, width_blk).transpose(1, 0, 2)
    cum = jnp.cumsum(decay, axis=2)
    last = cum[:, :, -1]

    tail = jnp.exp(last[:, :, None] - cum)
    key_decayed = k.astype(jnp.float32) * tail.transpose(0, 2, 1)[:, :, :, None]
    block_state = jnp.einsum(
        "bshd,bshe->bhde", key_decayed, v.astype(jnp.float32), precision=hp
    )

    carries = []
    run = jnp.zeros((head_count, head_width, head_width), jnp.float32)
    before = jnp.zeros((head_count,), jnp.float32)
    offsets = []
    for b in range(blocks):
        carries.append(run)
        offsets.append(before)
        run = jnp.exp(last[b])[:, None, None] * run + block_state[b]
        before = before + last[b]
    local_state = run
    own_total = before

    incoming = exclusive_prefix(local_state, own_total, "ctx")

    lower = jnp.arange(width_blk)[:, None] >= jnp.arange(width_blk)[None, :]
    spread = cum[:, :, :, None] - cum[:, :, None, :]
    factor = jnp.exp(jnp.where(lower[None, None], spread, -jnp.inf))
    scores = jnp.einsum("bthd,bshd->bhts", q, k, preferred_element_type=jnp.float32)
    weighted = (scores * factor).astype(jnp.bfloat16)
    inside = jnp.einsum("bhts,bshd->bthd", weighted, v, preferred_element_type=jnp.float32)

    carry_all = jnp.stack(
        [carries[b] + jnp.exp(offsets[b])[:, None, None] * incoming for b in range(blocks)]
    )
    carried = jnp.exp(cum).transpose(0, 2, 1)[:, :, :, None] * jnp.einsum(
        "bthd,bhde->bthe", q.astype(jnp.float32), carry_all, precision=hp
    )
    attn = (inside + carried).reshape(local_rows, head_count, head_width)

    tp = lax.axis_size("tp")
    chunks = 2
    sub = local_rows // tp // chunks
    attn = attn.reshape(tp, chunks, sub, head_count, head_width)
    gate_all = gates.reshape(tp, chunks, sub, head_count, head_width)
    gain = norm_gain.reshape(head_count, head_width)
    outs = []
    for c in range(chunks):
        part = attn[:, c]
        meansq = jnp.mean(part * part, axis=-1, keepdims=True)
        gate = jax.nn.sigmoid(gate_all[:, c].astype(jnp.float32))
        normed = part * lax.rsqrt(meansq + 1e-06) * gain * gate
        normed = normed.astype(jnp.bfloat16).reshape(tp * sub, head_count * head_width)
        outs.append(
            lax.psum_scatter(
                jnp.dot(normed, out_weight, preferred_element_type=jnp.float32).astype(
                    jnp.bfloat16
                ),
                "tp",
                scatter_dimension=0,
                tiled=True,
            )
        )
    return jnp.concatenate(outs, axis=0)


def solution(mesh):
    placed = (
        P("ctx", "tp"),
        P("ctx", "tp"),
        P("ctx", "tp"),
        P("ctx", "tp"),
        P("tp", "ctx"),
        P("tp"),
        P("tp", None),
    )
    return jax.shard_map(
        on_device, mesh=mesh, in_specs=placed, out_specs=P(("ctx", "tp"), None), check_vma=False
    )
```

```python
import jax
import jax.numpy as jnp
from jax import lax
from jax.sharding import PartitionSpec as P


def exclusive_prefix(state, total, axis, group):
    n = lax.axis_size(axis)
    me = lax.axis_index(axis)
    heads, rows, cols = state.shape
    pad = 8

    def pack(st, tot):
        hi = tot.astype(jnp.bfloat16)
        lo = (tot - hi.astype(jnp.float32)).astype(jnp.bfloat16)
        parts = jnp.stack([hi, lo] + [jnp.zeros_like(hi)] * (pad - 2), axis=1)
        return jnp.concatenate(
            [st.astype(jnp.bfloat16), jnp.broadcast_to(parts[:, :, None], (heads, pad, cols))],
            axis=1,
        )

    def unpack(x):
        x = x.astype(jnp.float32)
        return x[:, :rows, :], x[:, rows, 0] + x[:, rows + 1, 0]

    def level(st, tot, stride, count):
        digit = (me // stride) % count
        sts, tots = [st], [tot]
        sent = pack(st, tot)
        for d in range(1, count):
            got_st, got_tot = unpack(
                lax.ppermute(sent, axis, [(i, i ^ (d * stride)) for i in range(n)])
            )
            sts.append(got_st)
            tots.append(got_tot)
        tots = jnp.stack(tots)
        pos = jnp.arange(count) ^ digit
        earlier = pos[:, None] < pos[None, :]
        is_before = pos < digit
        mask_b = earlier & is_before[None, :]
        w_before = jnp.where(
            is_before[:, None],
            jnp.exp(jnp.sum(jnp.where(mask_b[:, :, None], tots[None], 0.0), axis=1)),
            0.0,
        )
        w_whole = jnp.exp(jnp.sum(jnp.where(earlier[:, :, None], tots[None], 0.0), axis=1))
        before = sum(w_before[d][:, None, None] * sts[d] for d in range(count))
        whole = sum(w_whole[d][:, None, None] * sts[d] for d in range(count))
        tot_before = jnp.sum(jnp.where(is_before[:, None], tots, 0.0), axis=0)
        tot_whole = jnp.sum(tots, axis=0)
        return (before, tot_before), (whole, tot_whole)

    (in_st, in_tot), (row_st, row_tot) = level(state, total, 1, group)
    if group == n:
        return in_st
    (out_st, _), _ = level(row_st, row_tot, group, n // group)
    return jnp.exp(in_tot)[:, None, None] * out_st + in_st


def on_device(queries, keys, values, gates, log_decay, norm_gain, out_weight):
    local_rows = queries.shape[0]
    head_count = log_decay.shape[0]
    head_width = queries.shape[1] // head_count
    width_blk = min(local_rows, 512)
    blocks = local_rows // width_blk
    hp = lax.Precision.HIGHEST

    q = queries.reshape(blocks, width_blk, head_count, head_width)
    k = keys.reshape(blocks, width_blk, head_count, head_width)
    v = values.reshape(blocks, width_blk, head_count, head_width)
    decay = log_decay.reshape(head_count, blocks, width_blk).transpose(1, 0, 2)
    cum = jnp.cumsum(decay, axis=2)
    last = cum[:, :, -1]

    tail = jnp.exp(last[:, :, None] - cum)
    key_decayed = k.astype(jnp.float32) * tail.transpose(0, 2, 1)[:, :, :, None]
    block_state = jnp.einsum(
        "bshd,bshe->bhde", key_decayed, v.astype(jnp.float32), precision=hp
    )

    carries = []
    run = jnp.zeros((head_count, head_width, head_width), jnp.float32)
    before = jnp.zeros((head_count,), jnp.float32)
    offsets = []
    for b in range(blocks):
        carries.append(run)
        offsets.append(before)
        run = jnp.exp(last[b])[:, None, None] * run + block_state[b]
        before = before + last[b]
    local_state = run
    own_total = before

    ctx_size = lax.axis_size("ctx")
    group = 8 if ctx_size % 8 == 0 else ctx_size
    incoming = exclusive_prefix(local_state, own_total, "ctx", group)

    lower = jnp.arange(width_blk)[:, None] >= jnp.arange(width_blk)[None, :]
    spread = cum[:, :, :, None] - cum[:, :, None, :]
    factor = jnp.exp(jnp.where(lower[None, None], spread, -jnp.inf))
    scores = jnp.einsum("bthd,bshd->bhts", q, k, preferred_element_type=jnp.float32)
    weighted = (scores * factor).astype(jnp.bfloat16)
    inside = jnp.einsum("bhts,bshd->bthd", weighted, v, preferred_element_type=jnp.float32)

    carry_all = jnp.stack(
        [carries[b] + jnp.exp(offsets[b])[:, None, None] * incoming for b in range(blocks)]
    )
    carried = jnp.exp(cum).transpose(0, 2, 1)[:, :, :, None] * jnp.einsum(
        "bthd,bhde->bthe", q.astype(jnp.float32), carry_all, precision=hp
    )
    attn = (inside + carried).reshape(local_rows, head_count, head_width)

    meansq = jnp.mean(attn * attn, axis=-1, keepdims=True)
    gate = jax.nn.sigmoid(gates.reshape(local_rows, head_count, head_width).astype(jnp.float32))
    normed = attn * lax.rsqrt(meansq + 1e-06) * norm_gain.reshape(head_count, head_width) * gate
    normed = normed.astype(jnp.bfloat16).reshape(local_rows, head_count * head_width)
    return lax.psum_scatter(
        jnp.dot(normed, out_weight, preferred_element_type=jnp.float32).astype(jnp.bfloat16),
        "tp",
        scatter_dimension=0,
        tiled=True,
    )


def solution(mesh):
    placed = (
        P("ctx", "tp"),
        P("ctx", "tp"),
        P("ctx", "tp"),
        P("ctx", "tp"),
        P("tp", "ctx"),
        P("tp"),
        P("tp", None),
    )
    return jax.shard_map(
        on_device, mesh=mesh, in_specs=placed, out_specs=P(("ctx", "tp"), None), check_vma=False
    )
```

```python
import jax
import jax.numpy as jnp
from jax import lax
from jax.sharding import PartitionSpec as P


def exclusive_prefix(state, total, axis, group):
    n = lax.axis_size(axis)
    me = lax.axis_index(axis)
    heads, rows, cols = state.shape
    pad = 8

    def pack(st, tot):
        hi = tot.astype(jnp.bfloat16)
        lo = (tot - hi.astype(jnp.float32)).astype(jnp.bfloat16)
        parts = jnp.stack([hi, lo] + [jnp.zeros_like(hi)] * (pad - 2), axis=1)
        return jnp.concatenate(
            [st.astype(jnp.bfloat16), jnp.broadcast_to(parts[:, :, None], (heads, pad, cols))],
            axis=1,
        )

    def unpack(x):
        x = x.astype(jnp.float32)
        return x[:, :rows, :], x[:, rows, 0] + x[:, rows + 1, 0]

    def join(earlier, later):
        return (jnp.exp(later[1])[:, None, None] * earlier[0] + later[0], earlier[1] + later[1])

    block = (state, total)
    prefix = (jnp.zeros_like(state), jnp.zeros_like(total))
    s = 1
    while s < n:
        flip = 2 * s - 1 if s < group else 2 * s - group
        other = unpack(lax.ppermute(pack(*block), axis, [(i, i ^ flip) for i in range(n)]))
        lower = (me & s) != 0
        new_prefix = join(other, prefix)
        prefix = tuple(jnp.where(lower, a, b) for a, b in zip(new_prefix, prefix))
        block = tuple(
            jnp.where(lower, a, b) for a, b in zip(join(other, block), join(block, other))
        )
        s *= 2
    return prefix[0]


def on_device(queries, keys, values, gates, log_decay, norm_gain, out_weight):
    local_rows = queries.shape[0]
    head_count = log_decay.shape[0]
    head_width = queries.shape[1] // head_count
    width_blk = min(local_rows, 512)
    blocks = local_rows // width_blk
    hp = lax.Precision.HIGHEST

    q = queries.reshape(blocks, width_blk, head_count, head_width)
    k = keys.reshape(blocks, width_blk, head_count, head_width)
    v = values.reshape(blocks, width_blk, head_count, head_width)
    decay = log_decay.reshape(head_count, blocks, width_blk).transpose(1, 0, 2)
    cum = jnp.cumsum(decay, axis=2)
    last = cum[:, :, -1]

    tail = jnp.exp(last[:, :, None] - cum)
    key_decayed = k.astype(jnp.float32) * tail.transpose(0, 2, 1)[:, :, :, None]
    block_state = jnp.einsum(
        "bshd,bshe->bhde", key_decayed, v.astype(jnp.float32), precision=hp
    )

    carries = []
    run = jnp.zeros((head_count, head_width, head_width), jnp.float32)
    before = jnp.zeros((head_count,), jnp.float32)
    offsets = []
    for b in range(blocks):
        carries.append(run)
        offsets.append(before)
        run = jnp.exp(last[b])[:, None, None] * run + block_state[b]
        before = before + last[b]

    later = (jnp.arange(local_rows)[:, None] > jnp.arange(local_rows)[None, :]).astype(jnp.float32)
    suffix = jnp.dot(log_decay, later, precision=hp)
    key_tail = keys.reshape(local_rows, head_count, head_width).astype(jnp.float32) * jnp.exp(
        suffix
    ).T[:, :, None]
    local_state = jnp.einsum(
        "shd,she->hde",
        key_tail,
        values.reshape(local_rows, head_count, head_width).astype(jnp.float32),
        precision=hp,
    )
    own_total = jnp.sum(log_decay, axis=1)
    ctx_size = lax.axis_size("ctx")
    group = 8 if ctx_size % 8 == 0 else ctx_size

    incoming = exclusive_prefix(local_state, own_total, "ctx", group)

    lower = jnp.arange(width_blk)[:, None] >= jnp.arange(width_blk)[None, :]
    spread = cum[:, :, :, None] - cum[:, :, None, :]
    factor = jnp.exp(jnp.where(lower[None, None], spread, -jnp.inf))
    scores = jnp.einsum("bthd,bshd->bhts", q, k, preferred_element_type=jnp.float32)
    weighted = (scores * factor).astype(jnp.bfloat16)
    inside = jnp.einsum("bhts,bshd->bthd", weighted, v, preferred_element_type=jnp.float32)

    carry_all = jnp.stack(
        [carries[b] + jnp.exp(offsets[b])[:, None, None] * incoming for b in range(blocks)]
    )
    carried = jnp.exp(cum).transpose(0, 2, 1)[:, :, :, None] * jnp.einsum(
        "bthd,bhde->bthe", q.astype(jnp.float32), carry_all, precision=hp
    )
    attn = (inside + carried).reshape(local_rows, head_count, head_width)

    meansq = jnp.mean(attn * attn, axis=-1, keepdims=True)
    gate = jax.nn.sigmoid(gates.reshape(local_rows, head_count, head_width).astype(jnp.float32))
    normed = attn * lax.rsqrt(meansq + 1e-06) * norm_gain.reshape(head_count, head_width) * gate
    normed = normed.astype(jnp.bfloat16).reshape(local_rows, head_count * head_width)
    return lax.psum_scatter(
        jnp.dot(normed, out_weight, preferred_element_type=jnp.float32).astype(jnp.bfloat16),
        "tp",
        scatter_dimension=0,
        tiled=True,
    )


def solution(mesh):
    placed = (
        P("ctx", "tp"),
        P("ctx", "tp"),
        P("ctx", "tp"),
        P("ctx", "tp"),
        P("tp", "ctx"),
        P("tp"),
        P("tp", None),
    )
    return jax.shard_map(
        on_device, mesh=mesh, in_specs=placed, out_specs=P(("ctx", "tp"), None), check_vma=False
    )
```

```python
import jax
import jax.numpy as jnp
from jax import lax
from jax.sharding import PartitionSpec as P


def exclusive_prefix(state, total, axis, group):
    n = lax.axis_size(axis)
    me = lax.axis_index(axis)
    heads, rows, cols = state.shape
    pad = 8

    def pack(st, tot):
        hi = tot.astype(jnp.bfloat16)
        lo = (tot - hi.astype(jnp.float32)).astype(jnp.bfloat16)
        parts = jnp.stack([hi, lo] + [jnp.zeros_like(hi)] * (pad - 2), axis=1)
        return jnp.concatenate(
            [st.astype(jnp.bfloat16), jnp.broadcast_to(parts[:, :, None], (heads, pad, cols))],
            axis=1,
        )

    def unpack(x):
        x = x.astype(jnp.float32)
        return x[:, :rows, :], x[:, rows, 0] + x[:, rows + 1, 0]

    def join(earlier, later):
        return (jnp.exp(later[1])[:, None, None] * earlier[0] + later[0], earlier[1] + later[1])

    block = (state, total)
    prefix = (jnp.zeros_like(state), jnp.zeros_like(total))
    s = 1
    while s < n:
        flip = 2 * s - 1 if s < group else 2 * s - group
        other = unpack(lax.ppermute(pack(*block), axis, [(i, i ^ flip) for i in range(n)]))
        lower = (me & s) != 0
        new_prefix = join(other, prefix)
        prefix = tuple(jnp.where(lower, a, b) for a, b in zip(new_prefix, prefix))
        block = tuple(
            jnp.where(lower, a, b) for a, b in zip(join(other, block), join(block, other))
        )
        s *= 2
    return prefix[0]


def on_device(queries, keys, values, gates, log_decay, norm_gain, out_weight):
    local_rows = queries.shape[0]
    head_count = log_decay.shape[0]
    head_width = queries.shape[1] // head_count
    width_blk = min(local_rows, 512)
    blocks = local_rows // width_blk
    hp = lax.Precision.HIGHEST

    q = queries.reshape(blocks, width_blk, head_count, head_width)
    k = keys.reshape(blocks, width_blk, head_count, head_width)
    v = values.reshape(blocks, width_blk, head_count, head_width)
    decay = log_decay.reshape(head_count, blocks, width_blk).transpose(1, 0, 2)
    cum = jnp.cumsum(decay, axis=2)
    last = cum[:, :, -1]

    tail = jnp.exp(last[:, :, None] - cum)
    key_decayed = k.astype(jnp.float32) * tail.transpose(0, 2, 1)[:, :, :, None]
    block_state = jnp.einsum(
        "bshd,bshe->bhde", key_decayed, v.astype(jnp.float32), precision=hp
    )

    carries = []
    run = jnp.zeros((head_count, head_width, head_width), jnp.float32)
    before = jnp.zeros((head_count,), jnp.float32)
    offsets = []
    for b in range(blocks):
        carries.append(run)
        offsets.append(before)
        run = jnp.exp(last[b])[:, None, None] * run + block_state[b]
        before = before + last[b]
    local_state = run
    own_total = before

    ctx_size = lax.axis_size("ctx")
    group = 8 if ctx_size % 8 == 0 else ctx_size
    incoming = exclusive_prefix(local_state, own_total, "ctx", group)

    lower = jnp.arange(width_blk)[:, None] >= jnp.arange(width_blk)[None, :]
    spread = cum[:, :, :, None] - cum[:, :, None, :]
    factor = jnp.exp(jnp.where(lower[None, None], spread, -jnp.inf))
    scores = jnp.einsum("bthd,bshd->bhts", q, k, preferred_element_type=jnp.float32)
    weighted = (scores * factor).astype(jnp.bfloat16)
    inside = jnp.einsum("bhts,bshd->bthd", weighted, v, preferred_element_type=jnp.float32)

    carry_all = jnp.stack(
        [carries[b] + jnp.exp(offsets[b])[:, None, None] * incoming for b in range(blocks)]
    )
    carried = jnp.exp(cum).transpose(0, 2, 1)[:, :, :, None] * jnp.einsum(
        "bthd,bhde->bthe", q.astype(jnp.float32), carry_all, precision=hp
    )
    attn = (inside + carried).reshape(local_rows, head_count, head_width)

    meansq = jnp.mean(attn * attn, axis=-1, keepdims=True)
    gate = jax.nn.sigmoid(gates.reshape(local_rows, head_count, head_width).astype(jnp.float32))
    normed = attn * lax.rsqrt(meansq + 1e-06) * norm_gain.reshape(head_count, head_width) * gate
    normed = normed.astype(jnp.bfloat16).reshape(local_rows, head_count * head_width)
    return lax.psum_scatter(
        jnp.dot(normed, out_weight, preferred_element_type=jnp.float32).astype(jnp.bfloat16),
        "tp",
        scatter_dimension=0,
        tiled=True,
    )


def solution(mesh):
    placed = (
        P("ctx", "tp"),
        P("ctx", "tp"),
        P("ctx", "tp"),
        P("ctx", "tp"),
        P("tp", "ctx"),
        P("tp"),
        P("tp", None),
    )
    return jax.shard_map(
        on_device, mesh=mesh, in_specs=placed, out_specs=P(("ctx", "tp"), None), check_vma=False
    )
```

```python
import jax
import jax.numpy as jnp
from jax import lax
from jax.sharding import PartitionSpec as P


def exclusive_prefix(state, total, axis, group):
    n = lax.axis_size(axis)
    me = lax.axis_index(axis)
    heads, rows, cols = state.shape
    pad = 8

    def pack(st, tot):
        hi = tot.astype(jnp.bfloat16)
        lo = (tot - hi.astype(jnp.float32)).astype(jnp.bfloat16)
        parts = jnp.stack([hi, lo] + [jnp.zeros_like(hi)] * (pad - 2), axis=1)
        return jnp.concatenate(
            [st.astype(jnp.bfloat16), jnp.broadcast_to(parts[:, :, None], (heads, pad, cols))],
            axis=1,
        )

    def unpack(x):
        x = x.astype(jnp.float32)
        return x[:, :rows, :], x[:, rows, 0] + x[:, rows + 1, 0]

    def join(earlier, later):
        return (jnp.exp(later[1])[:, None, None] * earlier[0] + later[0], earlier[1] + later[1])

    block = (state, total)
    prefix = (jnp.zeros_like(state), jnp.zeros_like(total))
    s = 1
    while s < n:
        flip = 2 * s - 1 if s < group else 2 * s - group
        other = unpack(lax.ppermute(pack(*block), axis, [(i, i ^ flip) for i in range(n)]))
        lower = (me & s) != 0
        new_prefix = join(other, prefix)
        prefix = tuple(jnp.where(lower, a, b) for a, b in zip(new_prefix, prefix))
        block = tuple(
            jnp.where(lower, a, b) for a, b in zip(join(other, block), join(block, other))
        )
        s *= 2
    return prefix[0]


def on_device(queries, keys, values, gates, log_decay, norm_gain, out_weight):
    local_rows = queries.shape[0]
    head_count = log_decay.shape[0]
    head_width = queries.shape[1] // head_count
    width_blk = min(local_rows, 512)
    blocks = local_rows // width_blk
    hp = lax.Precision.HIGHEST

    q = queries.reshape(blocks, width_blk, head_count, head_width)
    k = keys.reshape(blocks, width_blk, head_count, head_width)
    v = values.reshape(blocks, width_blk, head_count, head_width)
    decay = log_decay.reshape(head_count, blocks, width_blk).transpose(1, 0, 2)
    cum = jnp.cumsum(decay, axis=2)
    last = cum[:, :, -1]

    tail = jnp.exp(last[:, :, None] - cum)
    key_decayed = k.astype(jnp.float32) * tail.transpose(0, 2, 1)[:, :, :, None]
    block_state = jnp.einsum(
        "bshd,bshe->bhde", key_decayed, v.astype(jnp.float32), precision=hp
    )

    carries = []
    run = jnp.zeros((head_count, head_width, head_width), jnp.float32)
    before = jnp.zeros((head_count,), jnp.float32)
    offsets = []
    for b in range(blocks):
        carries.append(run)
        offsets.append(before)
        run = jnp.exp(last[b])[:, None, None] * run + block_state[b]
        before = before + last[b]
    local_state = run
    own_total = before

    ctx_size = lax.axis_size("ctx")
    group = 8 if ctx_size % 8 == 0 else ctx_size
    incoming = exclusive_prefix(local_state, own_total, "ctx", group)

    lower = jnp.arange(width_blk)[:, None] >= jnp.arange(width_blk)[None, :]
    spread = cum[:, :, :, None] - cum[:, :, None, :]
    factor = jnp.exp(jnp.where(lower[None, None], spread, -jnp.inf))
    scores = jnp.einsum("bthd,bshd->bhts", q, k, preferred_element_type=jnp.float32)
    weighted = (scores * factor).astype(jnp.bfloat16)
    inside = jnp.einsum("bhts,bshd->bhtd", weighted, v, preferred_element_type=jnp.float32)

    carry_all = jnp.stack(
        [carries[b] + jnp.exp(offsets[b])[:, None, None] * incoming for b in range(blocks)]
    )
    carried = jnp.exp(cum)[:, :, :, None] * jnp.einsum(
        "bthd,bhde->bhte", q.astype(jnp.float32), carry_all, precision=hp
    )
    attn = inside + carried

    meansq = jnp.mean(attn * attn, axis=-1, keepdims=True)
    gate = jax.nn.sigmoid(
        gates.reshape(blocks, width_blk, head_count, head_width)
        .transpose(0, 2, 1, 3)
        .astype(jnp.float32)
    )
    normed = attn * lax.rsqrt(meansq + 1e-06) * norm_gain.reshape(head_count, 1, head_width) * gate
    normed = normed.astype(jnp.bfloat16)
    projected = jnp.einsum(
        "bhte,hen->btn",
        normed,
        out_weight.reshape(head_count, head_width, out_weight.shape[1]),
        preferred_element_type=jnp.float32,
    ).reshape(local_rows, out_weight.shape[1])
    return lax.psum_scatter(
        projected.astype(jnp.bfloat16), "tp", scatter_dimension=0, tiled=True
    )


def solution(mesh):
    placed = (
        P("ctx", "tp"),
        P("ctx", "tp"),
        P("ctx", "tp"),
        P("ctx", "tp"),
        P("tp", "ctx"),
        P("tp"),
        P("tp", None),
    )
    return jax.shard_map(
        on_device, mesh=mesh, in_specs=placed, out_specs=P(("ctx", "tp"), None), check_vma=False
    )
```

```python
import jax
import jax.numpy as jnp
from jax import lax
from jax.sharding import PartitionSpec as P


def exclusive_prefix(state, total, axis, group):
    n = lax.axis_size(axis)
    me = lax.axis_index(axis)
    heads, rows, cols = state.shape
    pad = 8

    def pack(st, tot):
        hi = tot.astype(jnp.bfloat16)
        lo = (tot - hi.astype(jnp.float32)).astype(jnp.bfloat16)
        parts = jnp.stack([hi, lo] + [jnp.zeros_like(hi)] * (pad - 2), axis=1)
        return jnp.concatenate(
            [st.astype(jnp.bfloat16), jnp.broadcast_to(parts[:, :, None], (heads, pad, cols))],
            axis=1,
        )

    def unpack(x):
        x = x.astype(jnp.float32)
        return x[:, :rows, :], x[:, rows, 0] + x[:, rows + 1, 0]

    def join(earlier, later):
        return (jnp.exp(later[1])[:, None, None] * earlier[0] + later[0], earlier[1] + later[1])

    block = (state, total)
    prefix = (jnp.zeros_like(state), jnp.zeros_like(total))
    s = 1
    while s < n:
        flip = 2 * s - 1 if s < group else 2 * s - group
        other = unpack(lax.ppermute(pack(*block), axis, [(i, i ^ flip) for i in range(n)]))
        lower = (me & s) != 0
        new_prefix = join(other, prefix)
        prefix = tuple(jnp.where(lower, a, b) for a, b in zip(new_prefix, prefix))
        block = tuple(
            jnp.where(lower, a, b) for a, b in zip(join(other, block), join(block, other))
        )
        s *= 2
    return prefix[0]


def on_device(queries, keys, values, gates, log_decay, norm_gain, out_weight):
    local_rows = queries.shape[0]
    head_count = log_decay.shape[0]
    head_width = queries.shape[1] // head_count
    width_blk = min(local_rows, 512)
    blocks = local_rows // width_blk
    hp = lax.Precision.HIGHEST

    q = queries.reshape(blocks, width_blk, head_count, head_width)
    k = keys.reshape(blocks, width_blk, head_count, head_width)
    v = values.reshape(blocks, width_blk, head_count, head_width)
    decay = log_decay.reshape(head_count, blocks, width_blk).transpose(1, 0, 2)
    upto = (jnp.arange(width_blk)[:, None] <= jnp.arange(width_blk)[None, :]).astype(jnp.float32)
    cum = jnp.einsum("bhu,ut->bht", decay, upto, precision=hp)
    last = cum[:, :, -1]

    tail = jnp.exp(last[:, :, None] - cum)
    key_decayed = k.astype(jnp.float32) * tail.transpose(0, 2, 1)[:, :, :, None]
    block_state = jnp.einsum(
        "bshd,bshe->bhde", key_decayed, v.astype(jnp.float32), precision=hp
    )

    carries = []
    run = jnp.zeros((head_count, head_width, head_width), jnp.float32)
    before = jnp.zeros((head_count,), jnp.float32)
    offsets = []
    for b in range(blocks):
        carries.append(run)
        offsets.append(before)
        run = jnp.exp(last[b])[:, None, None] * run + block_state[b]
        before = before + last[b]
    local_state = run
    own_total = before

    ctx_size = lax.axis_size("ctx")
    group = 8 if ctx_size % 8 == 0 else ctx_size
    incoming = exclusive_prefix(local_state, own_total, "ctx", group)

    lower = jnp.arange(width_blk)[:, None] >= jnp.arange(width_blk)[None, :]
    spread = cum[:, :, :, None] - cum[:, :, None, :]
    factor = jnp.exp(jnp.where(lower[None, None], spread, -jnp.inf))
    scores = jnp.einsum("bthd,bshd->bhts", q, k, preferred_element_type=jnp.float32)
    weighted = (scores * factor).astype(jnp.bfloat16)
    inside = jnp.einsum("bhts,bshd->bthd", weighted, v, preferred_element_type=jnp.float32)

    carry_all = jnp.stack(
        [carries[b] + jnp.exp(offsets[b])[:, None, None] * incoming for b in range(blocks)]
    )
    carried = jnp.exp(cum).transpose(0, 2, 1)[:, :, :, None] * jnp.einsum(
        "bthd,bhde->bthe", q.astype(jnp.float32), carry_all, precision=hp
    )
    attn = (inside + carried).reshape(local_rows, head_count, head_width)

    meansq = jnp.mean(attn * attn, axis=-1, keepdims=True)
    gate = jax.nn.sigmoid(gates.reshape(local_rows, head_count, head_width).astype(jnp.float32))
    normed = attn * lax.rsqrt(meansq + 1e-06) * norm_gain.reshape(head_count, head_width) * gate
    normed = normed.astype(jnp.bfloat16).reshape(local_rows, head_count * head_width)
    return lax.psum_scatter(
        jnp.dot(normed, out_weight, preferred_element_type=jnp.float32).astype(jnp.bfloat16),
        "tp",
        scatter_dimension=0,
        tiled=True,
    )


def solution(mesh):
    placed = (
        P("ctx", "tp"),
        P("ctx", "tp"),
        P("ctx", "tp"),
        P("ctx", "tp"),
        P("tp", "ctx"),
        P("tp"),
        P("tp", None),
    )
    return jax.shard_map(
        on_device, mesh=mesh, in_specs=placed, out_specs=P(("ctx", "tp"), None), check_vma=False
    )
```

```python
import jax
import jax.numpy as jnp
from jax import lax
from jax.sharding import PartitionSpec as P


def exclusive_prefix(state, total, axis, group):
    n = lax.axis_size(axis)
    me = lax.axis_index(axis)
    heads, rows, cols = state.shape
    pad = 8

    def pack(st, tot):
        hi = tot.astype(jnp.bfloat16)
        lo = (tot - hi.astype(jnp.float32)).astype(jnp.bfloat16)
        parts = jnp.stack([hi, lo] + [jnp.zeros_like(hi)] * (pad - 2), axis=1)
        return jnp.concatenate(
            [st.astype(jnp.bfloat16), jnp.broadcast_to(parts[:, :, None], (heads, pad, cols))],
            axis=1,
        )

    def unpack(x):
        x = x.astype(jnp.float32)
        return x[:, :rows, :], x[:, rows, 0] + x[:, rows + 1, 0]

    def join(earlier, later):
        return (jnp.exp(later[1])[:, None, None] * earlier[0] + later[0], earlier[1] + later[1])

    block = (state, total)
    prefix = (jnp.zeros_like(state), jnp.zeros_like(total))
    s = 1
    while s < n:
        flip = 2 * s - 1 if s < group else 2 * s - group
        other = unpack(lax.ppermute(pack(*block), axis, [(i, i ^ flip) for i in range(n)]))
        lower = (me & s) != 0
        new_prefix = join(other, prefix)
        prefix = tuple(jnp.where(lower, a, b) for a, b in zip(new_prefix, prefix))
        block = tuple(
            jnp.where(lower, a, b) for a, b in zip(join(other, block), join(block, other))
        )
        s *= 2
    return prefix[0]


def split_dot(spec, a, b, lhs_wide):
    wide, narrow = (a, b) if lhs_wide else (b, a)
    hi = wide.astype(jnp.bfloat16)
    lo = (wide - hi.astype(jnp.float32)).astype(jnp.bfloat16)
    out = 0.0
    for part in (hi, lo):
        x, y = (part, narrow) if lhs_wide else (narrow, part)
        out = out + jnp.einsum(spec, x, y, preferred_element_type=jnp.float32)
    return out


def on_device(queries, keys, values, gates, log_decay, norm_gain, out_weight):
    local_rows = queries.shape[0]
    head_count = log_decay.shape[0]
    head_width = queries.shape[1] // head_count
    width_blk = min(local_rows, 512)
    blocks = local_rows // width_blk
    hp = lax.Precision.HIGHEST

    q = queries.reshape(blocks, width_blk, head_count, head_width)
    k = keys.reshape(blocks, width_blk, head_count, head_width)
    v = values.reshape(blocks, width_blk, head_count, head_width)
    decay = log_decay.reshape(head_count, blocks, width_blk).transpose(1, 0, 2)
    upto = (jnp.arange(width_blk)[:, None] <= jnp.arange(width_blk)[None, :]).astype(jnp.float32)
    cum = jnp.einsum("bhu,ut->bht", decay, upto, precision=hp)
    last = cum[:, :, -1]

    tail = jnp.exp(last[:, :, None] - cum)
    key_decayed = k.astype(jnp.float32) * tail.transpose(0, 2, 1)[:, :, :, None]
    block_state = split_dot("bshd,bshe->bhde", key_decayed, v, lhs_wide=True)

    carries = []
    run = jnp.zeros((head_count, head_width, head_width), jnp.float32)
    before = jnp.zeros((head_count,), jnp.float32)
    offsets = []
    for b in range(blocks):
        carries.append(run)
        offsets.append(before)
        run = jnp.exp(last[b])[:, None, None] * run + block_state[b]
        before = before + last[b]
    local_state = run
    own_total = before

    ctx_size = lax.axis_size("ctx")
    group = 8 if ctx_size % 8 == 0 else ctx_size
    incoming = exclusive_prefix(local_state, own_total, "ctx", group)

    lower = jnp.arange(width_blk)[:, None] >= jnp.arange(width_blk)[None, :]
    spread = cum[:, :, :, None] - cum[:, :, None, :]
    factor = jnp.exp(jnp.where(lower[None, None], spread, -jnp.inf))
    scores = jnp.einsum("bthd,bshd->bhts", q, k, preferred_element_type=jnp.float32)
    weighted = (scores * factor).astype(jnp.bfloat16)
    inside = jnp.einsum("bhts,bshd->bthd", weighted, v, preferred_element_type=jnp.float32)

    carry_all = jnp.stack(
        [carries[b] + jnp.exp(offsets[b])[:, None, None] * incoming for b in range(blocks)]
    )
    carried = jnp.exp(cum).transpose(0, 2, 1)[:, :, :, None] * split_dot("bthd,bhde->bthe", q, carry_all, lhs_wide=False)
    attn = (inside + carried).reshape(local_rows, head_count, head_width)

    meansq = jnp.mean(attn * attn, axis=-1, keepdims=True)
    gate = jax.nn.sigmoid(gates.reshape(local_rows, head_count, head_width).astype(jnp.float32))
    normed = attn * lax.rsqrt(meansq + 1e-06) * norm_gain.reshape(head_count, head_width) * gate
    normed = normed.astype(jnp.bfloat16).reshape(local_rows, head_count * head_width)
    return lax.psum_scatter(
        jnp.dot(normed, out_weight, preferred_element_type=jnp.float32).astype(jnp.bfloat16),
        "tp",
        scatter_dimension=0,
        tiled=True,
    )


def solution(mesh):
    placed = (
        P("ctx", "tp"),
        P("ctx", "tp"),
        P("ctx", "tp"),
        P("ctx", "tp"),
        P("tp", "ctx"),
        P("tp"),
        P("tp", None),
    )
    return jax.shard_map(
        on_device, mesh=mesh, in_specs=placed, out_specs=P(("ctx", "tp"), None), check_vma=False
    )
```

```python
import jax
import jax.numpy as jnp
from jax import lax
from jax.sharding import PartitionSpec as P


def exclusive_prefix(state, total, axis, group):
    n = lax.axis_size(axis)
    me = lax.axis_index(axis)
    heads, rows, cols = state.shape
    pad = 8

    def pack(st, tot):
        hi = tot.astype(jnp.bfloat16)
        lo = (tot - hi.astype(jnp.float32)).astype(jnp.bfloat16)
        parts = jnp.stack([hi, lo] + [jnp.zeros_like(hi)] * (pad - 2), axis=1)
        return jnp.concatenate(
            [st.astype(jnp.bfloat16), jnp.broadcast_to(parts[:, :, None], (heads, pad, cols))],
            axis=1,
        )

    def unpack(x):
        x = x.astype(jnp.float32)
        return x[:, :rows, :], x[:, rows, 0] + x[:, rows + 1, 0]

    def join(earlier, later):
        return (jnp.exp(later[1])[:, None, None] * earlier[0] + later[0], earlier[1] + later[1])

    block = (state, total)
    prefix = (jnp.zeros_like(state), jnp.zeros_like(total))
    s = 1
    while s < n:
        flip = 2 * s - 1 if s < group else 2 * s - group
        other = unpack(lax.ppermute(pack(*block), axis, [(i, i ^ flip) for i in range(n)]))
        lower = (me & s) != 0
        new_prefix = join(other, prefix)
        prefix = tuple(jnp.where(lower, a, b) for a, b in zip(new_prefix, prefix))
        block = tuple(
            jnp.where(lower, a, b) for a, b in zip(join(other, block), join(block, other))
        )
        s *= 2
    return prefix[0]


def on_device(queries, keys, values, gates, log_decay, norm_gain, out_weight):
    local_rows = queries.shape[0]
    head_count = log_decay.shape[0]
    head_width = queries.shape[1] // head_count
    width_blk = min(local_rows, 512)
    blocks = local_rows // width_blk
    hp = lax.Precision.HIGHEST

    q = queries.reshape(blocks, width_blk, head_count, head_width)
    k = keys.reshape(blocks, width_blk, head_count, head_width)
    v = values.reshape(blocks, width_blk, head_count, head_width)
    decay = log_decay.reshape(head_count, blocks, width_blk).transpose(1, 0, 2)
    upto = (jnp.arange(width_blk)[:, None] <= jnp.arange(width_blk)[None, :]).astype(jnp.float32)
    cum = jnp.einsum("bhu,ut->bht", decay, upto, precision=hp)
    last = cum[:, :, -1]

    tail = jnp.exp(last[:, :, None] - cum)
    key_decayed = k.astype(jnp.float32) * tail.transpose(0, 2, 1)[:, :, :, None]
    block_state = jnp.einsum(
        "bshd,bshe->bhde", key_decayed, v.astype(jnp.float32), precision=lax.Precision.HIGH
    )

    carries = []
    run = jnp.zeros((head_count, head_width, head_width), jnp.float32)
    before = jnp.zeros((head_count,), jnp.float32)
    offsets = []
    for b in range(blocks):
        carries.append(run)
        offsets.append(before)
        run = jnp.exp(last[b])[:, None, None] * run + block_state[b]
        before = before + last[b]
    local_state = run
    own_total = before

    ctx_size = lax.axis_size("ctx")
    group = 8 if ctx_size % 8 == 0 else ctx_size
    incoming = exclusive_prefix(local_state, own_total, "ctx", group)

    lower = jnp.arange(width_blk)[:, None] >= jnp.arange(width_blk)[None, :]
    spread = cum[:, :, :, None] - cum[:, :, None, :]
    factor = jnp.exp(jnp.where(lower[None, None], spread, -jnp.inf))
    scores = jnp.einsum("bthd,bshd->bhts", q, k, preferred_element_type=jnp.float32)
    weighted = (scores * factor).astype(jnp.bfloat16)
    inside = jnp.einsum("bhts,bshd->bthd", weighted, v, preferred_element_type=jnp.float32)

    carry_all = jnp.stack(
        [carries[b] + jnp.exp(offsets[b])[:, None, None] * incoming for b in range(blocks)]
    )
    carried = jnp.exp(cum).transpose(0, 2, 1)[:, :, :, None] * jnp.einsum(
        "bthd,bhde->bthe", q.astype(jnp.float32), carry_all, precision=lax.Precision.HIGH
    )
    attn = (inside + carried).reshape(local_rows, head_count, head_width)

    meansq = jnp.mean(attn * attn, axis=-1, keepdims=True)
    gate = jax.nn.sigmoid(gates.reshape(local_rows, head_count, head_width).astype(jnp.float32))
    normed = attn * lax.rsqrt(meansq + 1e-06) * norm_gain.reshape(head_count, head_width) * gate
    normed = normed.astype(jnp.bfloat16).reshape(local_rows, head_count * head_width)
    return lax.psum_scatter(
        jnp.dot(normed, out_weight, preferred_element_type=jnp.float32).astype(jnp.bfloat16),
        "tp",
        scatter_dimension=0,
        tiled=True,
    )


def solution(mesh):
    placed = (
        P("ctx", "tp"),
        P("ctx", "tp"),
        P("ctx", "tp"),
        P("ctx", "tp"),
        P("tp", "ctx"),
        P("tp"),
        P("tp", None),
    )
    return jax.shard_map(
        on_device, mesh=mesh, in_specs=placed, out_specs=P(("ctx", "tp"), None), check_vma=False
    )
```

```python
import jax
import jax.numpy as jnp
from jax import lax
from jax.sharding import PartitionSpec as P


def exclusive_prefix(state, total, axis, group):
    n = lax.axis_size(axis)
    me = lax.axis_index(axis)
    heads, rows, cols = state.shape
    pad = 8

    def pack(st, tot):
        hi = tot.astype(jnp.bfloat16)
        lo = (tot - hi.astype(jnp.float32)).astype(jnp.bfloat16)
        parts = jnp.stack([hi, lo] + [jnp.zeros_like(hi)] * (pad - 2), axis=1)
        return jnp.concatenate(
            [st.astype(jnp.bfloat16), jnp.broadcast_to(parts[:, :, None], (heads, pad, cols))],
            axis=1,
        )

    def unpack(x):
        x = x.astype(jnp.float32)
        return x[:, :rows, :], x[:, rows, 0] + x[:, rows + 1, 0]

    def join(earlier, later):
        return (jnp.exp(later[1])[:, None, None] * earlier[0] + later[0], earlier[1] + later[1])

    block = (state, total)
    prefix = (jnp.zeros_like(state), jnp.zeros_like(total))
    s = 1
    while s < n:
        flip = 2 * s - 1 if s < group else 2 * s - group
        other = unpack(lax.ppermute(pack(*block), axis, [(i, i ^ flip) for i in range(n)]))
        lower = (me & s) != 0
        new_prefix = join(other, prefix)
        prefix = tuple(jnp.where(lower, a, b) for a, b in zip(new_prefix, prefix))
        block = tuple(
            jnp.where(lower, a, b) for a, b in zip(join(other, block), join(block, other))
        )
        s *= 2
    return prefix[0]


def on_device(queries, keys, values, gates, log_decay, norm_gain, out_weight):
    local_rows = queries.shape[0]
    head_count = log_decay.shape[0]
    head_width = queries.shape[1] // head_count
    width_blk = min(local_rows, 512)
    blocks = local_rows // width_blk
    hp = lax.Precision.HIGHEST

    q = queries.reshape(blocks, width_blk, head_count, head_width)
    k = keys.reshape(blocks, width_blk, head_count, head_width)
    v = values.reshape(blocks, width_blk, head_count, head_width)
    decay = log_decay.reshape(head_count, blocks, width_blk).transpose(1, 0, 2)
    upto = (jnp.arange(width_blk)[:, None] <= jnp.arange(width_blk)[None, :]).astype(jnp.bfloat16)
    cum = 0.0
    rest = decay
    for _ in range(3):
        part = rest.astype(jnp.bfloat16)
        rest = rest - part.astype(jnp.float32)
        cum = cum + jnp.einsum("bhu,ut->bht", part, upto, preferred_element_type=jnp.float32)
    last = cum[:, :, -1]

    tail = jnp.exp(last[:, :, None] - cum)
    key_decayed = k.astype(jnp.float32) * tail.transpose(0, 2, 1)[:, :, :, None]
    block_state = jnp.einsum(
        "bshd,bshe->bhde", key_decayed, v.astype(jnp.float32), precision=lax.Precision.HIGH
    )

    carries = []
    run = jnp.zeros((head_count, head_width, head_width), jnp.float32)
    before = jnp.zeros((head_count,), jnp.float32)
    offsets = []
    for b in range(blocks):
        carries.append(run)
        offsets.append(before)
        run = jnp.exp(last[b])[:, None, None] * run + block_state[b]
        before = before + last[b]
    local_state = run
    own_total = before

    ctx_size = lax.axis_size("ctx")
    group = 8 if ctx_size % 8 == 0 else ctx_size
    incoming = exclusive_prefix(local_state, own_total, "ctx", group)

    lower = jnp.arange(width_blk)[:, None] >= jnp.arange(width_blk)[None, :]
    spread = cum[:, :, :, None] - cum[:, :, None, :]
    factor = jnp.exp(jnp.where(lower[None, None], spread, -jnp.inf))
    scores = jnp.einsum("bthd,bshd->bhts", q, k, preferred_element_type=jnp.float32)
    weighted = (scores * factor).astype(jnp.bfloat16)
    inside = jnp.einsum("bhts,bshd->bthd", weighted, v, preferred_element_type=jnp.float32)

    carry_all = jnp.stack(
        [carries[b] + jnp.exp(offsets[b])[:, None, None] * incoming for b in range(blocks)]
    )
    carried = jnp.exp(cum).transpose(0, 2, 1)[:, :, :, None] * jnp.einsum(
        "bthd,bhde->bthe", q.astype(jnp.float32), carry_all, precision=lax.Precision.HIGH
    )
    attn = (inside + carried).reshape(local_rows, head_count, head_width)

    meansq = jnp.mean(attn * attn, axis=-1, keepdims=True)
    gate = jax.nn.sigmoid(gates.reshape(local_rows, head_count, head_width).astype(jnp.float32))
    normed = attn * lax.rsqrt(meansq + 1e-06) * norm_gain.reshape(head_count, head_width) * gate
    normed = normed.astype(jnp.bfloat16).reshape(local_rows, head_count * head_width)
    return lax.psum_scatter(
        jnp.dot(normed, out_weight, preferred_element_type=jnp.float32).astype(jnp.bfloat16),
        "tp",
        scatter_dimension=0,
        tiled=True,
    )


def solution(mesh):
    placed = (
        P("ctx", "tp"),
        P("ctx", "tp"),
        P("ctx", "tp"),
        P("ctx", "tp"),
        P("tp", "ctx"),
        P("tp"),
        P("tp", None),
    )
    return jax.shard_map(
        on_device, mesh=mesh, in_specs=placed, out_specs=P(("ctx", "tp"), None), check_vma=False
    )
```
